1024 devices in a mesh: batch: 8 (over z), seq: 8 (over x), head: 16 (over y, core).
Axes of the slice: x: 8, y: 8, z: 8, core: 2. Of those that a mesh axis runs over, the one named last changes fastest.
Arguments:
- queries: bfloat16 [40960, 8192], P(('batch', 'seq', 'head')), parts along dimension 0, may hold values from -6 to 6
- keys: bfloat16 [40960, 8192], P(('batch', 'seq', 'head')), parts along dimension 0, may hold values from -6 to 6
- values: bfloat16 [40960, 8192], P(('batch', 'seq', 'head')), parts along dimension 0, may hold values from -6 to 6
- group_order: int32 [64, 2], P(('batch', 'seq')), parts along dimension 0, may hold values from 0 to 15, as said below
- gain: float32 [8192], P('head'), may hold values from 0.1 to 1.9
Outputs:
- attended: bfloat16 [40960, 8192], P(('batch', 'seq'), 'head'), parts along dimension 0
The draws below stay inside these ranges and needn't reach their ends.
There are 8 independent parts, one for each index of `batch`. The reference program is written for one: setup_inputs(seed, part) draws one part's arguments, and reference() takes and returns one part's arrays. A program takes and returns all parts, laid end to end along the dimension named above; an argument that names none is the same for every part. Nothing has to cross between parts.
Inputs may be any that keep to these rules, and one draw needn't show every extreme that they name: `group_order`: row d holds d and 15 - d, in either order.
All inputs are finite; a program needn't handle non-finite values.
Results may differ from the reference program's by a relative error of at most 0.01.
Values may be sent and summed in bfloat16 or wider, within the bound.
No kernel may reach another device: no remote copies, remote signals or barrier semaphores. Data moves between devices by JAX's collectives and lax.ppermute only.
A program may use at most 32 MiB of HBM per device.

```python
import jax
import jax.numpy as jnp
from jax import lax

HEADS = 64
DH = 128
TOK_DEV = 640
PAIRS = 8
LENGTH = 5120
HD = 8192


def draw_group_order(key, part):
    flips = jax.random.randint(key, (PAIRS,), 0, 2)
    rows = jnp.arange(PAIRS, dtype=jnp.int32)
    mirror = 2 * PAIRS - 1 - rows
    first = jnp.where(flips == 1, mirror, rows)
    second = jnp.where(flips == 1, rows, mirror)
    return jnp.stack([first, second], axis=1).astype(jnp.int32)


def levels(stream_key, dims, split, smallest, high):
    def one(axis_at, parts):
        steps = jax.random.uniform(jax.random.fold_in(jax.random.fold_in(stream_key, 6), axis_at), (parts,), jnp.float32, smallest / len(split), high / len(split))
        return jnp.repeat(jnp.exp(steps), dims[axis_at] // parts).reshape((-1,) + (1,) * (len(dims) - axis_at - 1))

    level = one(*split[0])
    for cut in split[1:]:
        level = level * one(*cut)
    return level


def noise(rng, shape, deviation, reach, shards=(), kind=jnp.bfloat16):
    loudness = levels(rng, shape, shards, -0.22, 0.18) if shards else 1.0
    entries = jax.random.normal(rng, shape, jnp.float32) * deviation * loudness
    return jnp.minimum(jnp.maximum(entries, -reach), reach).astype(kind)


def setup_inputs(seed: int = 0, part: int = 0) -> dict:
    seeds = jax.random.split(jax.random.key(seed), 6)
    part_splits = jax.random.split(jax.random.fold_in(seeds[5], part), 6)
    queries = noise(part_splits[0], (LENGTH, HD), 1.0, 6.0, ((0, 128),))
    keys = noise(part_splits[1], (LENGTH, HD), 1.0, 6.0, ((0, 128),))
    values = noise(part_splits[2], (LENGTH, HD), 1.0, 6.0, ((0, 128),))
    group_order = draw_group_order(jax.random.fold_in(jax.random.fold_in(seeds[5], part), 71), part)
    gain = jnp.clip(1.0 + 0.18 * jax.random.normal(seeds[4], (HD,), jnp.float32), 0.1, 1.9)
    return dict(queries=queries, keys=keys, values=values, group_order=group_order, gain=gain)


def reference(queries, keys, values, group_order, gain):
    half = TOK_DEV // 2
    kc = keys.reshape(PAIRS, 2, half, HEADS, DH).astype(jnp.float32)
    vc = values.reshape(PAIRS, 2, half, HEADS, DH).astype(jnp.float32)
    state = jnp.einsum('cjthd,cjthe->cjhde', kc, vc).astype(jnp.bfloat16)
    state = lax.optimization_barrier(state).astype(jnp.float32)
    low_first = (group_order[:, 0] < PAIRS)[:, None, None, None]
    lows = jnp.where(low_first, state[:, 0], state[:, 1])
    highs = jnp.where(low_first, state[:, 1], state[:, 0])
    low_run = jnp.cumsum(lows, axis=0)
    high_run = jnp.cumsum(highs, axis=0)
    low_prefix = low_run - lows
    high_prefix = lax.optimization_barrier(jnp.sum(lows, axis=0)) - lows + (lax.optimization_barrier(jnp.sum(highs, axis=0)) - high_run)
    prefix = jnp.stack([jnp.where(low_first, low_prefix, high_prefix), jnp.where(low_first, high_prefix, low_prefix)], axis=1)
    prefix_b = prefix.astype(jnp.bfloat16).astype(jnp.float32)
    index = jnp.arange(TOK_DEV, dtype=jnp.int32)
    position = group_order[:, index // half] * half + index % half
    qb = queries.reshape(PAIRS, TOK_DEV, HEADS, DH)
    kb = keys.reshape(PAIRS, TOK_DEV, HEADS, DH)
    vb = values.reshape(PAIRS, TOK_DEV, HEADS, DH)
    gains = gain.reshape(HEADS, DH)

    def one_block(items):
        qx, kx, vx, pre, pos = items
        qf = qx.astype(jnp.float32)
        scores = jnp.einsum('thd,shd->hts', qf, kx.astype(jnp.float32))
        allowed = pos[:, None] >= pos[None, :]
        scores = jnp.where(allowed[None], scores, 0.0).astype(jnp.bfloat16)
        intra = jnp.einsum('hts,she->the', scores.astype(jnp.float32), vx.astype(jnp.float32))
        inter = jnp.einsum('jthd,jhde->jthe', qf.reshape(2, half, HEADS, DH), pre)
        raw = intra + inter.reshape(TOK_DEV, HEADS, DH)
        scale = lax.rsqrt(lax.optimization_barrier(jnp.mean(raw * raw, axis=-1, keepdims=True)) + 1e-06)
        return (raw * scale * gains).astype(jnp.bfloat16).reshape(TOK_DEV, HD)
    blocks = lax.map(one_block, (qb, kb, vb, prefix_b, position))
    return blocks.reshape(LENGTH, HD)
```

```python
import jax
import jax.numpy as jnp
from jax import lax
from jax.sharding import PartitionSpec as P

DH = 128


def local(queries, keys, values, group_order, gain):
    kv = jnp.stack([keys, values])
    kv_all = lax.all_to_all(kv, "head", split_axis=2, concat_axis=1, tiled=True)
    q_all = lax.all_to_all(queries, "head", split_axis=1, concat_axis=0, tiled=True)
    rows = q_all.shape[0]
    half = rows // 2
    local_heads = gain.shape[0] // DH
    pairs = lax.axis_size("seq")
    here = lax.axis_index("seq")
    qx = q_all.reshape(rows, local_heads, DH)
    kx = kv_all[0].reshape(rows, local_heads, DH)
    vx = kv_all[1].reshape(rows, local_heads, DH)
    kh = kx.reshape(2, half, local_heads, DH)
    vh = vx.reshape(2, half, local_heads, DH)
    state = jnp.einsum("jthd,jthe->jhde", kh, vh, preferred_element_type=jnp.float32).astype(
        jnp.bfloat16
    )
    order = group_order[0]
    low_first = order[0] < pairs
    lows = jnp.where(low_first, state[0], state[1])
    highs = jnp.where(low_first, state[1], state[0])
    both = (lows.astype(jnp.float32) + highs.astype(jnp.float32)).astype(jnp.bfloat16)
    owners = jnp.arange(pairs, dtype=jnp.int32)
    later = (owners > here)[:, None, None, None]
    send = jnp.where(later, lows[None], both[None])
    recv = lax.all_to_all(send, "seq", split_axis=0, concat_axis=0, tiled=True).astype(jnp.float32)
    below = (owners < here).astype(jnp.float32)[:, None, None, None]
    above = (owners > here).astype(jnp.float32)[:, None, None, None]
    low_sum = jnp.sum(recv * below, axis=0)
    high_sum = low_sum + jnp.sum(recv * above, axis=0)
    first_pre = jnp.where(low_first, low_sum, high_sum).astype(jnp.bfloat16)
    second_pre = jnp.where(low_first, high_sum, low_sum).astype(jnp.bfloat16)
    index = jnp.arange(rows, dtype=jnp.int32)
    position = order[index // half] * half + index % half
    scores = jnp.einsum("thd,shd->hts", qx, kx, preferred_element_type=jnp.float32)
    allowed = position[:, None] >= position[None, :]
    scores = jnp.where(allowed[None], scores, 0.0).astype(jnp.bfloat16)
    intra = jnp.einsum("hts,she->the", scores, vx, preferred_element_type=jnp.float32)
    qh = qx.reshape(2, half, local_heads, DH)
    first_term = jnp.einsum("thd,hde->the", qh[0], first_pre, preferred_element_type=jnp.float32)
    second_term = jnp.einsum("thd,hde->the", qh[1], second_pre, preferred_element_type=jnp.float32)
    raw = intra + jnp.concatenate([first_term, second_term], axis=0)
    scale = lax.rsqrt(jnp.mean(raw * raw, axis=-1, keepdims=True) + 1e-06)
    gains = gain.reshape(local_heads, DH)
    return (raw * scale * gains).astype(jnp.bfloat16).reshape(rows, local_heads * DH)


def solution(mesh):
    return jax.shard_map(
        local,
        mesh=mesh,
        in_specs=(
            P(("batch", "seq", "head"), None),
            P(("batch", "seq", "head"), None),
            P(("batch", "seq", "head"), None),
            P(("batch", "seq"), None),
            P("head"),
        ),
        out_specs=P(("batch", "seq"), "head"),
        check_vma=False,
    )
```

```python
import jax
import jax.numpy as jnp
from jax import lax
from jax.sharding import PartitionSpec as P

DH = 128


def local(queries, keys, values, group_order, gain):
    rows_in, feats = keys.shape
    ndev = lax.axis_size("head")
    width = feats // ndev

    def by_dest(x):
        return x.reshape(rows_in, ndev, width).transpose(1, 0, 2)

    kv = jnp.stack([by_dest(keys), by_dest(values)], axis=1).reshape(ndev, 2 * rows_in, width)
    kv_all = lax.all_to_all(kv, "head", split_axis=0, concat_axis=0, tiled=True)
    kv_all = kv_all.reshape(ndev, 2, rows_in, width)
    rows = ndev * rows_in
    half = rows // 2
    local_heads = gain.shape[0] // DH
    pairs = lax.axis_size("seq")
    here = lax.axis_index("seq")
    kx = kv_all[:, 0].reshape(rows, local_heads, DH)
    vx = kv_all[:, 1].reshape(rows, local_heads, DH)
    kh = kx.reshape(2, half, local_heads, DH)
    vh = vx.reshape(2, half, local_heads, DH)
    state = jnp.einsum("jthd,jthe->jhde", kh, vh, preferred_element_type=jnp.float32).astype(
        jnp.bfloat16
    )
    order = group_order[0]
    low_first = order[0] < pairs
    lows = jnp.where(low_first, state[0], state[1])
    highs = jnp.where(low_first, state[1], state[0])
    both = (lows.astype(jnp.float32) + highs.astype(jnp.float32)).astype(jnp.bfloat16)
    q_in, lows, both = lax.optimization_barrier((by_dest(queries), lows, both))
    q_all = lax.all_to_all(q_in, "head", split_axis=0, concat_axis=0, tiled=True)
    qx = q_all.reshape(rows, local_heads, DH)
    low_sum = jnp.zeros(lows.shape, jnp.float32)
    high_sum = jnp.zeros(lows.shape, jnp.float32)
    for shift in range(1, pairs):
        src = (here - shift) % pairs
        to = (here + shift) % pairs
        msg = jnp.where(to > here, lows, both)
        got = lax.ppermute(
            msg, "seq", [(i, (i + shift) % pairs) for i in range(pairs)]
        ).astype(jnp.float32)
        low_sum = low_sum + jnp.where(src < here, got, 0.0)
        high_sum = high_sum + got
    first_pre = jnp.where(low_first, low_sum, high_sum).astype(jnp.bfloat16)
    second_pre = jnp.where(low_first, high_sum, low_sum).astype(jnp.bfloat16)
    index = jnp.arange(rows, dtype=jnp.int32)
    position = order[index // half] * half + index % half
    scores = jnp.einsum("thd,shd->hts", qx, kx, preferred_element_type=jnp.float32)
    allowed = position[:, None] >= position[None, :]
    scores = jnp.where(allowed[None], scores, 0.0).astype(jnp.bfloat16)
    intra = jnp.einsum("hts,she->the", scores, vx, preferred_element_type=jnp.float32)
    qh = qx.reshape(2, half, local_heads, DH)
    first_term = jnp.einsum("thd,hde->the", qh[0], first_pre, preferred_element_type=jnp.float32)
    second_term = jnp.einsum("thd,hde->the", qh[1], second_pre, preferred_element_type=jnp.float32)
    raw = intra + jnp.concatenate([first_term, second_term], axis=0)
    scale = lax.rsqrt(jnp.mean(raw * raw, axis=-1, keepdims=True) + 1e-06)
    gains = gain.reshape(local_heads, DH)
    return (raw * scale * gains).astype(jnp.bfloat16).reshape(rows, local_heads * DH)


def solution(mesh):
    return jax.shard_map(
        local,
        mesh=mesh,
        in_specs=(
            P(("batch", "seq", "head"), None),
            P(("batch", "seq", "head"), None),
            P(("batch", "seq", "head"), None),
            P(("batch", "seq"), None),
            P("head"),
        ),
        out_specs=P(("batch", "seq"), "head"),
        check_vma=False,
    )
```

```python
import jax
import jax.numpy as jnp
from jax import lax
from jax.sharding import PartitionSpec as P

DH = 128


def exchange(lows, both, here, pairs):
    low_sum = jnp.zeros(lows.shape, jnp.float32)
    high_sum = jnp.zeros(lows.shape, jnp.float32)
    for shift in range(1, pairs):
        src = (here - shift) % pairs
        to = (here + shift) % pairs
        msg = jnp.where(to > here, lows, both)
        got = lax.ppermute(
            msg, "seq", [(i, (i + shift) % pairs) for i in range(pairs)]
        ).astype(jnp.float32)
        low_sum = low_sum + jnp.where(src < here, got, 0.0)
        high_sum = high_sum + got
    return low_sum, high_sum


def local(queries, keys, values, group_order, gain):
    rows_in, feats = keys.shape
    ndev = lax.axis_size("head")
    width = feats // ndev
    local_heads = gain.shape[0] // DH
    groups = 2
    gh = local_heads // groups
    rows = ndev * rows_in
    half = rows // 2
    pairs = lax.axis_size("seq")
    here = lax.axis_index("seq")
    order = group_order[0]
    low_first = order[0] < pairs

    def by_dest(x):
        return x.reshape(rows_in, ndev, width).transpose(1, 0, 2)

    kd = by_dest(keys).reshape(ndev, rows_in, groups, gh * DH)
    vd = by_dest(values).reshape(ndev, rows_in, groups, gh * DH)
    tie = ()
    kx_parts, vx_parts, pre_parts = [], [], []
    for g in range(groups):
        kv = jnp.stack([kd[:, :, g], vd[:, :, g]], axis=1).reshape(ndev, 2 * rows_in, gh * DH)
        if tie:
            kv, tie = lax.optimization_barrier((kv, tie))
            pre_parts.append(exchange(*tie, here, pairs))
        kv_all = lax.all_to_all(kv, "head", split_axis=0, concat_axis=0, tiled=True)
        kv_all = kv_all.reshape(ndev, 2, rows_in, gh * DH)
        kx = kv_all[:, 0].reshape(rows, gh, DH)
        vx = kv_all[:, 1].reshape(rows, gh, DH)
        kx_parts.append(kx)
        vx_parts.append(vx)
        kh = kx.reshape(2, half, gh, DH)
        vh = vx.reshape(2, half, gh, DH)
        state = jnp.einsum("jthd,jthe->jhde", kh, vh, preferred_element_type=jnp.float32).astype(
            jnp.bfloat16
        )
        lows = jnp.where(low_first, state[0], state[1])
        highs = jnp.where(low_first, state[1], state[0])
        both = (lows.astype(jnp.float32) + highs.astype(jnp.float32)).astype(jnp.bfloat16)
        tie = (lows, both)
    q_in, tie = lax.optimization_barrier((by_dest(queries), tie))
    pre_parts.append(exchange(*tie, here, pairs))
    q_all = lax.all_to_all(q_in, "head", split_axis=0, concat_axis=0, tiled=True)
    qx = q_all.reshape(rows, local_heads, DH)
    kx = jnp.concatenate(kx_parts, axis=1)
    vx = jnp.concatenate(vx_parts, axis=1)
    low_sum = jnp.concatenate([p[0] for p in pre_parts], axis=0)
    high_sum = jnp.concatenate([p[1] for p in pre_parts], axis=0)
    first_pre = jnp.where(low_first, low_sum, high_sum).astype(jnp.bfloat16)
    second_pre = jnp.where(low_first, high_sum, low_sum).astype(jnp.bfloat16)
    index = jnp.arange(rows, dtype=jnp.int32)
    position = order[index // half] * half + index % half
    scores = jnp.einsum("thd,shd->hts", qx, kx, preferred_element_type=jnp.float32)
    allowed = position[:, None] >= position[None, :]
    scores = jnp.where(allowed[None], scores, 0.0).astype(jnp.bfloat16)
    intra = jnp.einsum("hts,she->the", scores, vx, preferred_element_type=jnp.float32)
    qh = qx.reshape(2, half, local_heads, DH)
    first_term = jnp.einsum("thd,hde->the", qh[0], first_pre, preferred_element_type=jnp.float32)
    second_term = jnp.einsum("thd,hde->the", qh[1], second_pre, preferred_element_type=jnp.float32)
    raw = intra + jnp.concatenate([first_term, second_term], axis=0)
    scale = lax.rsqrt(jnp.mean(raw * raw, axis=-1, keepdims=True) + 1e-06)
    gains = gain.reshape(local_heads, DH)
    return (raw * scale * gains).astype(jnp.bfloat16).reshape(rows, local_heads * DH)


def solution(mesh):
    return jax.shard_map(
        local,
        mesh=mesh,
        in_specs=(
            P(("batch", "seq", "head"), None),
            P(("batch", "seq", "head"), None),
            P(("batch", "seq", "head"), None),
            P(("batch", "seq"), None),
            P("head"),
        ),
        out_specs=P(("batch", "seq"), "head"),
        check_vma=False,
    )
```

```python
import jax
import jax.numpy as jnp
from jax import lax
from jax.sharding import PartitionSpec as P

DH = 128


def exchange(lows, both, here, pairs):
    up = lows.astype(jnp.float32)
    down = both.astype(jnp.float32)
    step = 1
    while step < pairs:
        if 2 * step == pairs:
            msg = jnp.where(here + step < pairs, up, down).astype(jnp.bfloat16)
            got = lax.ppermute(
                msg, "seq", [(i, (i + step) % pairs) for i in range(pairs)]
            ).astype(jnp.float32)
            up = up + jnp.where(here >= step, got, 0.0)
            down = down + jnp.where(here + step < pairs, got, 0.0)
        else:
            got_up = lax.ppermute(
                up.astype(jnp.bfloat16), "seq", [(i, i + step) for i in range(pairs - step)]
            )
            got_down = lax.ppermute(
                down.astype(jnp.bfloat16), "seq", [(i, i - step) for i in range(step, pairs)]
            )
            up = up + got_up.astype(jnp.float32)
            down = down + got_down.astype(jnp.float32)
        step *= 2
    low_sum = up - lows.astype(jnp.float32)
    high_sum = low_sum + (down - both.astype(jnp.float32))
    return low_sum, high_sum


def local(queries, keys, values, group_order, gain):
    rows_in, feats = keys.shape
    ndev = lax.axis_size("head")
    width = feats // ndev
    local_heads = gain.shape[0] // DH
    groups = 1
    gh = local_heads // groups
    rows = ndev * rows_in
    half = rows // 2
    pairs = lax.axis_size("seq")
    here = lax.axis_index("seq")
    order = group_order[0]
    low_first = order[0] < pairs

    def by_dest(x):
        return x.reshape(rows_in, ndev, width).transpose(1, 0, 2)

    kd = by_dest(keys).reshape(ndev, rows_in, groups, gh * DH)
    vd = by_dest(values).reshape(ndev, rows_in, groups, gh * DH)
    tie = ()
    kx_parts, vx_parts, pre_parts = [], [], []
    for g in range(groups):
        kv = jnp.stack([kd[:, :, g], vd[:, :, g]], axis=1).reshape(ndev, 2 * rows_in, gh * DH)
        if tie:
            kv, tie = lax.optimization_barrier((kv, tie))
            pre_parts.append(exchange(*tie, here, pairs))
        kv_all = lax.all_to_all(kv, "head", split_axis=0, concat_axis=0, tiled=True)
        kv_all = kv_all.reshape(ndev, 2, rows_in, gh * DH)
        kx = kv_all[:, 0].reshape(rows, gh, DH)
        vx = kv_all[:, 1].reshape(rows, gh, DH)
        kx_parts.append(kx)
        vx_parts.append(vx)
        kh = kx.reshape(2, half, gh, DH)
        vh = vx.reshape(2, half, gh, DH)
        state = jnp.einsum("jthd,jthe->jhde", kh, vh, preferred_element_type=jnp.float32).astype(
            jnp.bfloat16
        )
        lows = jnp.where(low_first, state[0], state[1])
        highs = jnp.where(low_first, state[1], state[0])
        both = (lows.astype(jnp.float32) + highs.astype(jnp.float32)).astype(jnp.bfloat16)
        tie = (lows, both)
    q_in, tie = lax.optimization_barrier((by_dest(queries), tie))
    pre_parts.append(exchange(*tie, here, pairs))
    q_all = lax.all_to_all(q_in, "head", split_axis=0, concat_axis=0, tiled=True)
    qx = q_all.reshape(rows, local_heads, DH)
    kx = jnp.concatenate(kx_parts, axis=1)
    vx = jnp.concatenate(vx_parts, axis=1)
    low_sum = jnp.concatenate([p[0] for p in pre_parts], axis=0)
    high_sum = jnp.concatenate([p[1] for p in pre_parts], axis=0)
    first_pre = jnp.where(low_first, low_sum, high_sum).astype(jnp.bfloat16)
    second_pre = jnp.where(low_first, high_sum, low_sum).astype(jnp.bfloat16)
    index = jnp.arange(rows, dtype=jnp.int32)
    position = order[index // half] * half + index % half
    scores = jnp.einsum("thd,shd->hts", qx, kx, preferred_element_type=jnp.float32)
    allowed = position[:, None] >= position[None, :]
    scores = jnp.where(allowed[None], scores, 0.0).astype(jnp.bfloat16)
    intra = jnp.einsum("hts,she->the", scores, vx, preferred_element_type=jnp.float32)
    intra = lax.optimization_barrier(intra)
    qh = qx.reshape(2, half, local_heads, DH)
    first_term = jnp.einsum("thd,hde->the", qh[0], first_pre, preferred_element_type=jnp.float32)
    second_term = jnp.einsum("thd,hde->the", qh[1], second_pre, preferred_element_type=jnp.float32)
    raw = intra + jnp.concatenate([first_term, second_term], axis=0)
    scale = lax.rsqrt(jnp.mean(raw * raw, axis=-1, keepdims=True) + 1e-06)
    gains = gain.reshape(local_heads, DH)
    return (raw * scale * gains).astype(jnp.bfloat16).reshape(rows, local_heads * DH)


def solution(mesh):
    return jax.shard_map(
        local,
        mesh=mesh,
        in_specs=(
            P(("batch", "seq", "head"), None),
            P(("batch", "seq", "head"), None),
            P(("batch", "seq", "head"), None),
            P(("batch", "seq"), None),
            P("head"),
        ),
        out_specs=P(("batch", "seq"), "head"),
        check_vma=False,
    )
```

```python
import jax
import jax.numpy as jnp
from jax import lax
from jax.sharding import PartitionSpec as P

DH = 128


def exchange(lows, both, here, pairs):
    up = lows.astype(jnp.float32)
    down = both.astype(jnp.float32)
    reach = pairs // 2
    for step in range(1, reach):
        got_up = lax.ppermute(lows, "seq", [(i, i + step) for i in range(pairs - step)])
        got_down = lax.ppermute(both, "seq", [(i, i - step) for i in range(step, pairs)])
        up = up + got_up.astype(jnp.float32)
        down = down + got_down.astype(jnp.float32)
    step = reach
    while step < pairs:
        if 2 * step == pairs:
            msg = jnp.where(here + step < pairs, up, down).astype(jnp.bfloat16)
            got = lax.ppermute(
                msg, "seq", [(i, (i + step) % pairs) for i in range(pairs)]
            ).astype(jnp.float32)
            up = up + jnp.where(here >= step, got, 0.0)
            down = down + jnp.where(here + step < pairs, got, 0.0)
        else:
            got_up = lax.ppermute(
                up.astype(jnp.bfloat16), "seq", [(i, i + step) for i in range(pairs - step)]
            )
            got_down = lax.ppermute(
                down.astype(jnp.bfloat16), "seq", [(i, i - step) for i in range(step, pairs)]
            )
            up = up + got_up.astype(jnp.float32)
            down = down + got_down.astype(jnp.float32)
        step *= 2
    low_sum = up - lows.astype(jnp.float32)
    high_sum = low_sum + (down - both.astype(jnp.float32))
    return low_sum, high_sum


def local(queries, keys, values, group_order, gain):
    rows_in, feats = keys.shape
    ndev = lax.axis_size("head")
    width = feats // ndev
    local_heads = gain.shape[0] // DH
    groups = 1
    gh = local_heads // groups
    rows = ndev * rows_in
    half = rows // 2
    pairs = lax.axis_size("seq")
    here = lax.axis_index("seq")
    order = group_order[0]
    low_first = order[0] < pairs

    def by_dest(x):
        return x.reshape(rows_in, ndev, width).transpose(1, 0, 2)

    kd = by_dest(keys).reshape(ndev, rows_in, groups, gh * DH)
    vd = by_dest(values).reshape(ndev, rows_in, groups, gh * DH)
    tie = ()
    kx_parts, vx_parts, pre_parts = [], [], []
    for g in range(groups):
        kv = jnp.stack([kd[:, :, g], vd[:, :, g]], axis=1).reshape(ndev, 2 * rows_in, gh * DH)
        if tie:
            kv, tie = lax.optimization_barrier((kv, tie))
            pre_parts.append(exchange(*tie, here, pairs))
        kv_all = lax.all_to_all(kv, "head", split_axis=0, concat_axis=0, tiled=True)
        kv_all = kv_all.reshape(ndev, 2, rows_in, gh * DH)
        kx = kv_all[:, 0].reshape(rows, gh, DH)
        vx = kv_all[:, 1].reshape(rows, gh, DH)
        kx_parts.append(kx)
        vx_parts.append(vx)
        kh = kx.reshape(2, half, gh, DH)
        vh = vx.reshape(2, half, gh, DH)
        state = jnp.einsum("jthd,jthe->jhde", kh, vh, preferred_element_type=jnp.float32).astype(
            jnp.bfloat16
        )
        lows = jnp.where(low_first, state[0], state[1])
        highs = jnp.where(low_first, state[1], state[0])
        both = (lows.astype(jnp.float32) + highs.astype(jnp.float32)).astype(jnp.bfloat16)
        tie = (lows, both)
    q_in, tie = lax.optimization_barrier((by_dest(queries), tie))
    pre_parts.append(exchange(*tie, here, pairs))
    q_all = lax.all_to_all(q_in, "head", split_axis=0, concat_axis=0, tiled=True)
    qx = q_all.reshape(rows, local_heads, DH)
    kx = jnp.concatenate(kx_parts, axis=1)
    vx = jnp.concatenate(vx_parts, axis=1)
    low_sum = jnp.concatenate([p[0] for p in pre_parts], axis=0)
    high_sum = jnp.concatenate([p[1] for p in pre_parts], axis=0)
    first_pre = jnp.where(low_first, low_sum, high_sum).astype(jnp.bfloat16)
    second_pre = jnp.where(low_first, high_sum, low_sum).astype(jnp.bfloat16)
    index = jnp.arange(rows, dtype=jnp.int32)
    position = order[index // half] * half + index % half
    scores = jnp.einsum("thd,shd->hts", qx, kx, preferred_element_type=jnp.float32)
    allowed = position[:, None] >= position[None, :]
    scores = jnp.where(allowed[None], scores, 0.0).astype(jnp.bfloat16)
    intra = jnp.einsum("hts,she->the", scores, vx, preferred_element_type=jnp.float32)
    intra = lax.optimization_barrier(intra)
    qh = qx.reshape(2, half, local_heads, DH)
    first_term = jnp.einsum("thd,hde->the", qh[0], first_pre, preferred_element_type=jnp.float32)
    second_term = jnp.einsum("thd,hde->the", qh[1], second_pre, preferred_element_type=jnp.float32)
    raw = intra + jnp.concatenate([first_term, second_term], axis=0)
    scale = lax.rsqrt(jnp.mean(raw * raw, axis=-1, keepdims=True) + 1e-06)
    gains = gain.reshape(local_heads, DH)
    return (raw * scale * gains).astype(jnp.bfloat16).reshape(rows, local_heads * DH)


def solution(mesh):
    return jax.shard_map(
        local,
        mesh=mesh,
        in_specs=(
            P(("batch", "seq", "head"), None),
            P(("batch", "seq", "head"), None),
            P(("batch", "seq", "head"), None),
            P(("batch", "seq"), None),
            P("head"),
        ),
        out_specs=P(("batch", "seq"), "head"),
        check_vma=False,
    )
```

```python
import jax
import jax.numpy as jnp
from jax import lax
from jax.sharding import PartitionSpec as P

DH = 128


def exchange(lows, both, here, pairs):
    up = lows.astype(jnp.float32)
    down = both.astype(jnp.float32)
    step = pairs // 2
    msg = jnp.where(here + step < pairs, lows, both)
    got = lax.ppermute(
        msg, "seq", [(i, (i + step) % pairs) for i in range(pairs)]
    ).astype(jnp.float32)
    up = up + jnp.where(here >= step, got, 0.0)
    down = down + jnp.where(here + step < pairs, got, 0.0)
    step //= 2
    while step >= 1:
        got_up = lax.ppermute(
            up.astype(jnp.bfloat16), "seq", [(i, i + step) for i in range(pairs - step)]
        )
        got_down = lax.ppermute(
            down.astype(jnp.bfloat16), "seq", [(i, i - step) for i in range(step, pairs)]
        )
        up = up + got_up.astype(jnp.float32)
        down = down + got_down.astype(jnp.float32)
        step //= 2
    low_sum = up - lows.astype(jnp.float32)
    high_sum = low_sum + (down - both.astype(jnp.float32))
    return low_sum, high_sum


def local(queries, keys, values, group_order, gain):
    rows_in, feats = keys.shape
    ndev = lax.axis_size("head")
    width = feats // ndev
    local_heads = gain.shape[0] // DH
    groups = 1
    gh = local_heads // groups
    rows = ndev * rows_in
    half = rows // 2
    pairs = lax.axis_size("seq")
    here = lax.axis_index("seq")
    order = group_order[0]
    low_first = order[0] < pairs

    def by_dest(x):
        return x.reshape(rows_in, ndev, width).transpose(1, 0, 2)

    kd = by_dest(keys).reshape(ndev, rows_in, groups, gh * DH)
    vd = by_dest(values).reshape(ndev, rows_in, groups, gh * DH)
    tie = ()
    kx_parts, vx_parts, pre_parts = [], [], []
    for g in range(groups):
        kv = jnp.stack([kd[:, :, g], vd[:, :, g]], axis=1).reshape(ndev, 2 * rows_in, gh * DH)
        if tie:
            kv, tie = lax.optimization_barrier((kv, tie))
            pre_parts.append(exchange(*tie, here, pairs))
        kv_all = lax.all_to_all(kv, "head", split_axis=0, concat_axis=0, tiled=True)
        kv_all = kv_all.reshape(ndev, 2, rows_in, gh * DH)
        kx = kv_all[:, 0].reshape(rows, gh, DH)
        vx = kv_all[:, 1].reshape(rows, gh, DH)
        kx_parts.append(kx)
        vx_parts.append(vx)
        kh = kx.reshape(2, half, gh, DH)
        vh = vx.reshape(2, half, gh, DH)
        state = jnp.einsum("jthd,jthe->jhde", kh, vh, preferred_element_type=jnp.float32).astype(
            jnp.bfloat16
        )
        lows = jnp.where(low_first, state[0], state[1])
        highs = jnp.where(low_first, state[1], state[0])
        both = (lows.astype(jnp.float32) + highs.astype(jnp.float32)).astype(jnp.bfloat16)
        tie = (lows, both)
    q_in, tie = lax.optimization_barrier((by_dest(queries), tie))
    pre_parts.append(exchange(*tie, here, pairs))
    q_all = lax.all_to_all(q_in, "head", split_axis=0, concat_axis=0, tiled=True)
    qx = q_all.reshape(rows, local_heads, DH)
    kx = jnp.concatenate(kx_parts, axis=1)
    vx = jnp.concatenate(vx_parts, axis=1)
    low_sum = jnp.concatenate([p[0] for p in pre_parts], axis=0)
    high_sum = jnp.concatenate([p[1] for p in pre_parts], axis=0)
    first_pre = jnp.where(low_first, low_sum, high_sum).astype(jnp.bfloat16)
    second_pre = jnp.where(low_first, high_sum, low_sum).astype(jnp.bfloat16)
    index = jnp.arange(rows, dtype=jnp.int32)
    position = order[index // half] * half + index % half
    scores = jnp.einsum("thd,shd->hts", qx, kx, preferred_element_type=jnp.float32)
    allowed = position[:, None] >= position[None, :]
    scores = jnp.where(allowed[None], scores, 0.0).astype(jnp.bfloat16)
    intra = jnp.einsum("hts,she->the", scores, vx, preferred_element_type=jnp.float32)
    intra = lax.optimization_barrier(intra)
    qh = qx.reshape(2, half, local_heads, DH)
    first_term = jnp.einsum("thd,hde->the", qh[0], first_pre, preferred_element_type=jnp.float32)
    second_term = jnp.einsum("thd,hde->the", qh[1], second_pre, preferred_element_type=jnp.float32)
    raw = intra + jnp.concatenate([first_term, second_term], axis=0)
    scale = lax.rsqrt(jnp.mean(raw * raw, axis=-1, keepdims=True) + 1e-06)
    gains = gain.reshape(local_heads, DH)
    return (raw * scale * gains).astype(jnp.bfloat16).reshape(rows, local_heads * DH)


def solution(mesh):
    return jax.shard_map(
        local,
        mesh=mesh,
        in_specs=(
            P(("batch", "seq", "head"), None),
            P(("batch", "seq", "head"), None),
            P(("batch", "seq", "head"), None),
            P(("batch", "seq"), None),
            P("head"),
        ),
        out_specs=P(("batch", "seq"), "head"),
        check_vma=False,
    )
```

```python
import jax
import jax.numpy as jnp
from jax import lax
from jax.sharding import PartitionSpec as P

DH = 128


def exchange(lows, both, here, pairs):
    up = lows.astype(jnp.float32)
    down = both.astype(jnp.float32)
    got_up = lax.ppermute(lows, "seq", [(i, i + 3) for i in range(pairs - 3)])
    got_down = lax.ppermute(both, "seq", [(i, i - 3) for i in range(3, pairs)])
    msg = jnp.where(here + 6 < pairs, lows, both)
    far = [(i, i + 6) for i in range(pairs - 6)] + [(i, i - 6) for i in range(6, pairs)]
    got_far = lax.ppermute(msg, "seq", far).astype(jnp.float32)
    up = up + got_up.astype(jnp.float32) + jnp.where(here >= 6, got_far, 0.0)
    down = down + got_down.astype(jnp.float32) + jnp.where(here + 6 < pairs, got_far, 0.0)
    sent_up = up.astype(jnp.bfloat16)
    sent_down = down.astype(jnp.bfloat16)
    for step in (1, 2):
        got_up = lax.ppermute(sent_up, "seq", [(i, i + step) for i in range(pairs - step)])
        got_down = lax.ppermute(sent_down, "seq", [(i, i - step) for i in range(step, pairs)])
        up = up + got_up.astype(jnp.float32)
        down = down + got_down.astype(jnp.float32)
    low_sum = up - lows.astype(jnp.float32)
    high_sum = low_sum + (down - both.astype(jnp.float32))
    return low_sum, high_sum


def local(queries, keys, values, group_order, gain):
    rows_in, feats = keys.shape
    ndev = lax.axis_size("head")
    width = feats // ndev
    local_heads = gain.shape[0] // DH
    groups = 1
    gh = local_heads // groups
    rows = ndev * rows_in
    half = rows // 2
    pairs = lax.axis_size("seq")
    here = lax.axis_index("seq")
    order = group_order[0]
    low_first = order[0] < pairs

    def by_dest(x):
        return x.reshape(rows_in, ndev, width).transpose(1, 0, 2)

    kd = by_dest(keys).reshape(ndev, rows_in, groups, gh * DH)
    vd = by_dest(values).reshape(ndev, rows_in, groups, gh * DH)
    tie = ()
    kx_parts, vx_parts, pre_parts = [], [], []
    for g in range(groups):
        kv = jnp.stack([kd[:, :, g], vd[:, :, g]], axis=1).reshape(ndev, 2 * rows_in, gh * DH)
        if tie:
            kv, tie = lax.optimization_barrier((kv, tie))
            pre_parts.append(exchange(*tie, here, pairs))
        kv_all = lax.all_to_all(kv, "head", split_axis=0, concat_axis=0, tiled=True)
        kv_all = kv_all.reshape(ndev, 2, rows_in, gh * DH)
        kx = kv_all[:, 0].reshape(rows, gh, DH)
        vx = kv_all[:, 1].reshape(rows, gh, DH)
        kx_parts.append(kx)
        vx_parts.append(vx)
        kh = kx.reshape(2, half, gh, DH)
        vh = vx.reshape(2, half, gh, DH)
        state = jnp.einsum("jthd,jthe->jhde", kh, vh, preferred_element_type=jnp.float32).astype(
            jnp.bfloat16
        )
        lows = jnp.where(low_first, state[0], state[1])
        highs = jnp.where(low_first, state[1], state[0])
        both = (lows.astype(jnp.float32) + highs.astype(jnp.float32)).astype(jnp.bfloat16)
        tie = (lows, both)
    q_in, tie = lax.optimization_barrier((by_dest(queries), tie))
    pre_parts.append(exchange(*tie, here, pairs))
    q_all = lax.all_to_all(q_in, "head", split_axis=0, concat_axis=0, tiled=True)
    qx = q_all.reshape(rows, local_heads, DH)
    kx = jnp.concatenate(kx_parts, axis=1)
    vx = jnp.concatenate(vx_parts, axis=1)
    low_sum = jnp.concatenate([p[0] for p in pre_parts], axis=0)
    high_sum = jnp.concatenate([p[1] for p in pre_parts], axis=0)
    first_pre = jnp.where(low_first, low_sum, high_sum).astype(jnp.bfloat16)
    second_pre = jnp.where(low_first, high_sum, low_sum).astype(jnp.bfloat16)
    index = jnp.arange(rows, dtype=jnp.int32)
    position = order[index // half] * half + index % half
    scores = jnp.einsum("thd,shd->hts", qx, kx, preferred_element_type=jnp.float32)
    allowed = position[:, None] >= position[None, :]
    scores = jnp.where(allowed[None], scores, 0.0).astype(jnp.bfloat16)
    intra = jnp.einsum("hts,she->the", scores, vx, preferred_element_type=jnp.float32)
    intra = lax.optimization_barrier(intra)
    qh = qx.reshape(2, half, local_heads, DH)
    first_term = jnp.einsum("thd,hde->the", qh[0], first_pre, preferred_element_type=jnp.float32)
    second_term = jnp.einsum("thd,hde->the", qh[1], second_pre, preferred_element_type=jnp.float32)
    raw = intra + jnp.concatenate([first_term, second_term], axis=0)
    scale = lax.rsqrt(jnp.mean(raw * raw, axis=-1, keepdims=True) + 1e-06)
    gains = gain.reshape(local_heads, DH)
    return (raw * scale * gains).astype(jnp.bfloat16).reshape(rows, local_heads * DH)


def solution(mesh):
    return jax.shard_map(
        local,
        mesh=mesh,
        in_specs=(
            P(("batch", "seq", "head"), None),
            P(("batch", "seq", "head"), None),
            P(("batch", "seq", "head"), None),
            P(("batch", "seq"), None),
            P("head"),
        ),
        out_specs=P(("batch", "seq"), "head"),
        check_vma=False,
    )
```
